256 devices in a mesh: grp: 32 (over y, x, core), dev: 8 (over z).
Axes of the slice: x: 4, y: 4, z: 8, core: 2. Of those that a mesh axis runs over, the one named last changes fastest.
Arguments:
- rows: bfloat16 [524288, 1024], P(('grp', 'dev')), may hold values from -24 to 24
- lengths: int32 [32, 8], P('grp', 'dev'), may hold values from 1 to 2048, 8192 in all within a row
- sketch_block: int32 [524288], P(('grp', 'dev')), may hold values from 0 to 511
- sketch_sign: int32 [524288], P(('grp', 'dev')), may hold values from 0 to 1
Outputs:
- scores: float32 [524288], P(('grp', 'dev'))
The draws below stay inside these ranges and needn't reach their ends.
Inputs may be any that keep to these rules, and one draw needn't show every extreme that they name: The lengths of the 8 devices of one index of grp sum to 8192; the largest is 2048 in every such group.
All inputs are finite; a program needn't handle non-finite values.
Results may differ from the reference program's by a relative error of at most 0.00084.
Values may be sent and summed in bfloat16 or wider, within the bound.
No kernel may reach another device: no remote copies, remote signals or barrier semaphores. Data moves between devices by JAX's collectives and lax.ppermute only.
A program may use at most 128 MiB of HBM per device.

```python
import math
import jax
import jax.numpy as jnp
import numpy as np
from jax import lax

D = 1024
MEAN = 1024
CAP = 2048
SK_DEV = 512
ROWS = 524288
GROUP_ROWS = 8192
N_GRP = 32
N_DEV = 8


def with_ends(entries, stream_key, least, high):
    longest = entries.shape.index(max(entries.shape))
    spots = []
    for shift in (0, 1):
        where = [jax.random.randint(jax.random.fold_in(stream_key, axis), (), 0, length) for axis, length in enumerate(entries.shape)]
        where[longest] = (where[longest] + shift) % entries.shape[longest]
        spots.append(tuple(where))
    return entries.at[spots[0]].set(least).at[spots[1]].set(high)


def spiked(array, key, source, target, blocks, factor):
    def block_of(axis_at):
        return (jnp.arange(array.shape[axis_at]) // (array.shape[axis_at] // blocks)).reshape((-1,) + (1,) * (array.ndim - 1 - axis_at))

    first = jax.random.permutation(key, blocks)[block_of(target)]
    other_side = (block_of(target) + blocks // 2) % blocks
    return jnp.where((block_of(source) == first) | (block_of(source) == other_side), factor * array, array)


def block_scale(stream_key, dims, shards, low, largest):
    gain = 1.0
    for axis_at, blocks in shards:
        heights = jax.random.uniform(jax.random.fold_in(jax.random.fold_in(stream_key, 6), axis_at), (blocks,), jnp.float32, low / len(shards), largest / len(shards))
        gain = gain * jnp.repeat(jnp.exp(heights), dims[axis_at] // blocks).reshape((-1,) + (1,) * (len(dims) - 1 - axis_at))
    return gain


def split_up(number_of, total, reach, skew):
    loads = [(1 << 20) // math.isqrt(grade ** skew) + 1 for grade in range(2, number_of + 1)]
    surplus, given = total - reach - (number_of - 1), [1] * (number_of - 1)
    while surplus > 0:
        free = [i for i in range(number_of - 1) if given[i] < reach]
        mass, remaining = sum([loads[i] for i in free]), surplus
        for i in free:
            more = min(reach - given[i], max(1, remaining * loads[i] // mass), surplus)
            given[i] = given[i] + more
            surplus = surplus - more
    return np.array([reach] + given)


def uneven(stream_key, number_of, total, reach, skew):
    if number_of == 2:
        one = jax.random.randint(stream_key, (), max(1, total - reach), min(reach, total - 1) + 1)
        return jnp.stack([one, total - one])
    tallies = jnp.asarray(split_up(number_of, total, reach, skew), jnp.int32)
    couples = (number_of - 1) // 2
    source_of, receiver = tallies[1:1 + 2 * couples:2], tallies[2:2 + 2 * couples:2]
    room = jnp.minimum(source_of - 1, reach - receiver)
    shifted = jax.random.randint(jax.random.fold_in(stream_key, 1), (couples,), 0, 1 << 20) % (room + 1)
    tallies = tallies.at[1:1 + 2 * couples:2].set(source_of - shifted).at[2:2 + 2 * couples:2].set(receiver + shifted)
    return tallies[jax.random.permutation(jax.random.fold_in(stream_key, 2), number_of)]


def noise_with(key, dims, scale, limit, cuts, heavy, kind=jnp.bfloat16):
    result = scale * jax.random.normal(key, dims, jnp.float32)
    if cuts:
        result = result * block_scale(key, dims, cuts, -0.22, 0.18)
    return jnp.clip(spiked(result, jax.random.fold_in(key, 3), *heavy), -limit, limit).astype(kind)


def setup_inputs(seed: int = 0) -> dict:
    key_of = jax.random.split(jax.random.key(seed), 5)
    rows = noise_with(key_of[0], (ROWS, D), 1.0, 24.0, ((0, 256),), (0, 1, 256, 6.0))
    lengths = jax.vmap(lambda own: uneven(own, N_DEV, GROUP_ROWS, CAP, 2))(jax.random.split(key_of[1], N_GRP)).reshape((N_GRP, N_DEV)).astype(jnp.int32)
    sketch_block = with_ends(jax.random.randint(key_of[2], (ROWS,), 0, SK_DEV), jax.random.fold_in(key_of[2], 1), 0, SK_DEV - 1).astype(jnp.int32)
    sketch_sign = with_ends(jax.random.randint(key_of[3], (ROWS,), 0, 2), jax.random.fold_in(key_of[3], 1), 0, 1).astype(jnp.int32)
    return {"rows": rows, "lengths": lengths, "sketch_block": sketch_block, "sketch_sign": sketch_sign}


def reference(rows, lengths, sketch_block, sketch_sign):
    devices = N_GRP * N_DEV
    counts = lengths.reshape(devices)
    row_blocks = rows.reshape(devices, CAP, D)
    block_ids = sketch_block.reshape(devices, CAP)
    sign_bits = sketch_sign.reshape(devices, CAP)
    slot_index = jnp.arange(CAP, dtype=jnp.int32)

    def sketch_one(item):
        row_part, row_count, block_part, bit_part = item
        row_sign = jnp.where(slot_index < row_count, 2 * bit_part - 1, 0).astype(jnp.float32)
        summed = jax.ops.segment_sum(row_part.astype(jnp.float32) * row_sign[:, None], block_part, num_segments=SK_DEV)
        return summed.astype(jnp.bfloat16)
    sketched = lax.map(sketch_one, (row_blocks, counts, block_ids, sign_bits))

    def add_gram(running, sketch_part):
        widened = sketch_part.astype(jnp.float32)
        return (running + jnp.dot(widened.T, widened, precision=lax.Precision.HIGHEST), None)
    gram_matrix, unused = lax.scan(add_gram, jnp.zeros((D, D), jnp.float32), sketched)
    ridge_value = float(devices * MEAN)
    identity_matrix = jnp.eye(D, dtype=jnp.float32)
    lower_factor = jnp.linalg.cholesky(gram_matrix + ridge_value * identity_matrix)
    inverse = lax.linalg.triangular_solve(lower_factor, identity_matrix, left_side=True, lower=True)
    weight = inverse.T.astype(jnp.bfloat16)
    factor = ridge_value / D

    def score_one(item):
        row_part, row_count = item
        projected = jnp.dot(row_part.astype(jnp.float32), weight.astype(jnp.float32), preferred_element_type=jnp.float32)
        values = factor * jnp.sum(projected * projected, axis=1)
        return jnp.where(slot_index < row_count, values, jnp.zeros((), jnp.float32))
    return lax.map(score_one, (row_blocks, counts)).reshape(ROWS)
```

```python
import jax
import jax.numpy as jnp
from jax import lax
from jax.sharding import PartitionSpec as P

MEAN = 1024
SK_DEV = 512
BASE = 128
HI = lax.Precision.HIGHEST


def add_gram(row_piece):
    return lax.dot_general(
        row_piece, row_piece, (((0,), (0,)), ((), ())), preferred_element_type=jnp.float32
    )


def mm(a, b):
    return jnp.dot(a, b, precision=HI)


def mmt(a, b):
    return lax.dot_general(a, b, (((1,), (1,)), ((), ())), precision=HI)


def chol_inv(a):
    n = a.shape[0]
    if n <= BASE:
        lower = jnp.linalg.cholesky(a)
        eye = jnp.eye(n, dtype=jnp.float32)
        return lower, lax.linalg.triangular_solve(lower, eye, left_side=True, lower=True)
    h = n // 2
    l11, i11 = chol_inv(a[:h, :h])
    l21 = mmt(a[h:, :h], i11)
    l22, i22 = chol_inv(a[h:, h:] - mmt(l21, l21))
    i21 = -mm(i22, mm(l21, i11))
    z = jnp.zeros((h, n - h), jnp.float32)
    return jnp.block([[l11, z], [l21, l22]]), jnp.block([[i11, z], [i21, i22]])


def all_sum(g):
    n_dev = lax.axis_size("dev")
    n_grp = lax.axis_size("grp")
    rows, cols = g.shape
    part = lax.all_to_all(g.reshape(n_dev, rows // n_dev, cols), "dev", 0, 0, tiled=False).sum(0)
    piece = rows // (n_dev * n_grp)
    part = lax.all_to_all(part.reshape(n_grp, piece, cols), "grp", 0, 0, tiled=False).sum(0)
    part = lax.all_gather(part, "grp", axis=0, tiled=True)
    return lax.all_gather(part, "dev", axis=0, tiled=True)


def shards(rows, lengths, sketch_block, sketch_sign):
    capacity = rows.shape[0]
    features = rows.shape[1]
    row_count = lengths.reshape(())
    slot_index = lax.iota(jnp.int32, capacity)
    is_live = slot_index < row_count
    row_sign = jnp.where(is_live, 2 * sketch_sign - 1, 0).astype(jnp.bfloat16)
    picker = (lax.iota(jnp.int32, SK_DEV)[:, None] == sketch_block[None, :]).astype(
        jnp.bfloat16
    ) * row_sign[None, :]
    sketched = jnp.dot(picker, rows, preferred_element_type=jnp.float32).astype(jnp.bfloat16)
    gram_matrix = all_sum(add_gram(sketched))
    ridge_value = float(lax.axis_size("grp") * lax.axis_size("dev") * MEAN)
    identity_matrix = jnp.eye(features, dtype=jnp.float32)
    _, inverse = chol_inv(gram_matrix + ridge_value * identity_matrix)
    weight = inverse.T.astype(jnp.bfloat16)
    factor = ridge_value / features
    projected = jnp.dot(rows, weight, preferred_element_type=jnp.float32)
    return jnp.where(is_live, factor * jnp.sum(projected * projected, axis=1), 0.0)


def solution(mesh):
    in_specs = (P(("grp", "dev"), None), P("grp", "dev"), P(("grp", "dev")), P(("grp", "dev")))
    out_specs = P(("grp", "dev"))
    return jax.shard_map(shards, mesh=mesh, in_specs=in_specs, out_specs=out_specs, check_vma=False)
```

```python
import jax
import jax.numpy as jnp
from jax import lax
from jax.experimental import pallas as pl
from jax.experimental.pallas import tpu as pltpu
from jax.sharding import PartitionSpec as P

MEAN = 1024
SK_DEV = 512
BASE = 128
HI = lax.Precision.HIGHEST


def add_gram(row_piece):
    return lax.dot_general(
        row_piece, row_piece, (((0,), (0,)), ((), ())), preferred_element_type=jnp.float32
    )


def mm(a, b):
    return jnp.dot(a, b, precision=HI)


def mmt(a, b):
    return lax.dot_general(a, b, (((1,), (1,)), ((), ())), precision=HI)


def _base_kernel(a_ref, o_ref, m_ref):
    n = a_ref.shape[0]
    m_ref[:, :n] = a_ref[...]
    r = lax.broadcasted_iota(jnp.int32, (n, n), 0)
    c = lax.broadcasted_iota(jnp.int32, (n, n), 1)
    m_ref[:, n:] = jnp.where(r == c, 1.0, 0.0).astype(jnp.float32)

    def step(k, carry):
        row = m_ref[pl.ds(k, 1), :]
        lane = lax.broadcasted_iota(jnp.int32, (1, 2 * n), 1)
        piv = jnp.sum(jnp.where(lane == k, row, 0.0), axis=1, keepdims=True)
        s = 1.0 / jnp.sqrt(piv)
        rk = row * s
        m = m_ref[...]
        left_lane = lax.broadcasted_iota(jnp.int32, (n, n), 1)
        col = jnp.sum(jnp.where(left_lane == k, m[:, :n], 0.0), axis=1, keepdims=True)
        sub = lax.broadcasted_iota(jnp.int32, (n, 1), 0)
        mult = jnp.where(sub > k, col * s, 0.0)
        m_ref[...] = m - mult * rk
        m_ref[pl.ds(k, 1), :] = rk
        return carry

    lax.fori_loop(0, n, step, 0)
    o_ref[...] = m_ref[:, n:]


def base_inv(a):
    n = a.shape[0]
    return pl.pallas_call(
        _base_kernel,
        out_shape=jax.ShapeDtypeStruct((n, n), jnp.float32),
        scratch_shapes=[pltpu.VMEM((n, 2 * n), jnp.float32)],
    )(a)


def chol_inv(a):
    n = a.shape[0]
    if n <= BASE:
        return base_inv(a)
    h = n // 2
    i11 = chol_inv(a[:h, :h])
    l21 = mmt(a[h:, :h], i11)
    i22 = chol_inv(a[h:, h:] - mmt(l21, l21))
    i21 = -mm(i22, mm(l21, i11))
    z = jnp.zeros((h, n - h), jnp.float32)
    return jnp.block([[i11, z], [i21, i22]])


def all_sum(g):
    n_dev = lax.axis_size("dev")
    n_grp = lax.axis_size("grp")
    rows, cols = g.shape
    part = lax.all_to_all(g.reshape(n_grp, rows // n_grp, cols), "grp", 0, 0, tiled=False).sum(0)
    piece = rows // (n_dev * n_grp)
    part = lax.all_to_all(part.reshape(n_dev, piece, cols), "dev", 0, 0, tiled=False).sum(0)
    part = lax.all_gather(part, "dev", axis=0, tiled=True)
    return lax.all_gather(part, "grp", axis=0, tiled=True)


def shards(rows, lengths, sketch_block, sketch_sign):
    capacity = rows.shape[0]
    features = rows.shape[1]
    row_count = lengths.reshape(())
    slot_index = lax.iota(jnp.int32, capacity)
    is_live = slot_index < row_count
    row_sign = jnp.where(is_live, 2 * sketch_sign - 1, 0).astype(jnp.bfloat16)
    picker = (lax.iota(jnp.int32, SK_DEV)[:, None] == sketch_block[None, :]).astype(
        jnp.bfloat16
    ) * row_sign[None, :]
    sketched = jnp.dot(picker, rows, preferred_element_type=jnp.float32).astype(jnp.bfloat16)
    gram_matrix = all_sum(add_gram(sketched))
    ridge_value = float(lax.axis_size("grp") * lax.axis_size("dev") * MEAN)
    identity_matrix = jnp.eye(features, dtype=jnp.float32)
    inverse = chol_inv(gram_matrix + ridge_value * identity_matrix)
    weight = inverse.T.astype(jnp.bfloat16)
    factor = ridge_value / features
    projected = jnp.dot(rows, weight, preferred_element_type=jnp.float32)
    return jnp.where(is_live, factor * jnp.sum(projected * projected, axis=1), 0.0)


def solution(mesh):
    in_specs = (P(("grp", "dev"), None), P("grp", "dev"), P(("grp", "dev")), P(("grp", "dev")))
    out_specs = P(("grp", "dev"))
    return jax.shard_map(shards, mesh=mesh, in_specs=in_specs, out_specs=out_specs, check_vma=False)
```

```python
import jax
import jax.numpy as jnp
from jax import lax
from jax.experimental import pallas as pl
from jax.experimental.pallas import tpu as pltpu
from jax.sharding import PartitionSpec as P

MEAN = 1024
SK_DEV = 512
BASE = 128
GROUP = 8
HI = lax.Precision.HIGHEST


def add_gram(row_piece):
    return lax.dot_general(
        row_piece, row_piece, (((0,), (0,)), ((), ())), preferred_element_type=jnp.float32
    )


def mm(a, b):
    return jnp.dot(a, b, precision=HI)


def mmt(a, b):
    return lax.dot_general(a, b, (((1,), (1,)), ((), ())), precision=HI)


def _base_kernel(a_ref, o_ref, m_ref):
    n = a_ref.shape[0]
    m_ref[:, :n] = a_ref[...]
    r = lax.broadcasted_iota(jnp.int32, (n, n), 0)
    c = lax.broadcasted_iota(jnp.int32, (n, n), 1)
    m_ref[:, n:] = jnp.where(r == c, 1.0, 0.0).astype(jnp.float32)

    def make_step(lo):
        def step(k, carry):
            row = m_ref[pl.ds(k, 1), :]
            lane = lax.broadcasted_iota(jnp.int32, (1, 2 * n), 1)
            piv = jnp.sum(jnp.where(lane == k, row, 0.0), axis=1, keepdims=True)
            s = lax.rsqrt(piv)
            rk = row * s
            m = m_ref[lo:, :]
            left_lane = lax.broadcasted_iota(jnp.int32, (n - lo, n), 1)
            col = jnp.sum(jnp.where(left_lane == k, m[:, :n], 0.0), axis=1, keepdims=True)
            sub = lax.broadcasted_iota(jnp.int32, (n - lo, 1), 0) + lo
            mult = jnp.where(sub > k, col * s, 0.0)
            m_ref[lo:, :] = m - mult * rk
            m_ref[pl.ds(k, 1), :] = rk
            return carry

        return step

    for g in range(n // GROUP):
        lax.fori_loop(g * GROUP, (g + 1) * GROUP, make_step(g * GROUP), 0)
    o_ref[...] = m_ref[:, n:]


def base_inv(a):
    n = a.shape[0]
    return pl.pallas_call(
        _base_kernel,
        out_shape=jax.ShapeDtypeStruct((n, n), jnp.float32),
        scratch_shapes=[pltpu.VMEM((n, 2 * n), jnp.float32)],
    )(a)


def chol_inv(a):
    n = a.shape[0]
    if n <= BASE:
        return base_inv(a)
    h = n // 2
    i11 = chol_inv(a[:h, :h])
    l21 = mmt(a[h:, :h], i11)
    i22 = chol_inv(a[h:, h:] - mmt(l21, l21))
    i21 = -mm(i22, mm(l21, i11))
    z = jnp.zeros((h, n - h), jnp.float32)
    return jnp.block([[i11, z], [i21, i22]])


def all_sum(g):
    n_dev = lax.axis_size("dev")
    n_grp = lax.axis_size("grp")
    rows, cols = g.shape
    part = lax.all_to_all(g.reshape(n_grp, rows // n_grp, cols), "grp", 0, 0, tiled=False).sum(0)
    piece = rows // (n_dev * n_grp)
    part = lax.all_to_all(part.reshape(n_dev, piece, cols), "dev", 0, 0, tiled=False).sum(0)
    part = lax.all_gather(part, "dev", axis=0, tiled=True)
    return lax.all_gather(part, "grp", axis=0, tiled=True)


def shards(rows, lengths, sketch_block, sketch_sign):
    capacity = rows.shape[0]
    features = rows.shape[1]
    row_count = lengths.reshape(())
    slot_index = lax.iota(jnp.int32, capacity)
    is_live = slot_index < row_count
    row_sign = jnp.where(is_live, 2 * sketch_sign - 1, 0).astype(jnp.bfloat16)
    picker = (lax.iota(jnp.int32, SK_DEV)[:, None] == sketch_block[None, :]).astype(
        jnp.bfloat16
    ) * row_sign[None, :]
    sketched = jnp.dot(picker, rows, preferred_element_type=jnp.float32).astype(jnp.bfloat16)
    h = features // 2
    gram_left = all_sum(lax.dot_general(
        sketched, sketched[:, :h], (((0,), (0,)), ((), ())), preferred_element_type=jnp.float32
    ))
    gram_corner = all_sum(add_gram(sketched[:, h:]))
    ridge_value = float(lax.axis_size("grp") * lax.axis_size("dev") * MEAN)
    ridge = ridge_value * jnp.eye(h, dtype=jnp.float32)
    i11 = chol_inv(gram_left[:h] + ridge)
    l21 = mmt(gram_left[h:], i11)
    i22 = chol_inv(gram_corner + ridge - mmt(l21, l21))
    i21 = -mm(i22, mm(l21, i11))
    inverse = jnp.block([[i11, jnp.zeros((h, h), jnp.float32)], [i21, i22]])
    weight = inverse.T.astype(jnp.bfloat16)
    factor = ridge_value / features
    projected = jnp.dot(rows, weight, preferred_element_type=jnp.float32)
    return jnp.where(is_live, factor * jnp.sum(projected * projected, axis=1), 0.0)


def solution(mesh):
    in_specs = (P(("grp", "dev"), None), P("grp", "dev"), P(("grp", "dev")), P(("grp", "dev")))
    out_specs = P(("grp", "dev"))
    return jax.shard_map(shards, mesh=mesh, in_specs=in_specs, out_specs=out_specs, check_vma=False)
```

```python
import jax
import jax.numpy as jnp
from jax import lax
from jax.experimental import pallas as pl
from jax.experimental.pallas import tpu as pltpu
from jax.sharding import PartitionSpec as P

MEAN = 1024
SK_DEV = 512
BASE = 128
GROUP = 8
HI = lax.Precision.HIGHEST


def add_gram(row_piece):
    return lax.dot_general(
        row_piece, row_piece, (((0,), (0,)), ((), ())), preferred_element_type=jnp.float32
    )


def mm(a, b):
    return jnp.dot(a, b, precision=HI)


def mmt(a, b):
    return lax.dot_general(a, b, (((1,), (1,)), ((), ())), precision=HI)


def _base_kernel(a_ref, o_ref, m_ref):
    n = a_ref.shape[0]
    m_ref[:, :n] = a_ref[...]
    r = lax.broadcasted_iota(jnp.int32, (n, n), 0)
    c = lax.broadcasted_iota(jnp.int32, (n, n), 1)
    m_ref[:, n:] = jnp.where(r == c, 1.0, 0.0).astype(jnp.float32)

    def make_step(lo):
        def step(k, carry):
            row = m_ref[pl.ds(k, 1), :]
            lane = lax.broadcasted_iota(jnp.int32, (1, 2 * n), 1)
            piv = jnp.sum(jnp.where(lane == k, row, 0.0), axis=1, keepdims=True)
            s = lax.rsqrt(piv)
            rk = row * s
            m = m_ref[lo:, :]
            left_lane = lax.broadcasted_iota(jnp.int32, (n - lo, n), 1)
            col = jnp.sum(jnp.where(left_lane == k, m[:, :n], 0.0), axis=1, keepdims=True)
            sub = lax.broadcasted_iota(jnp.int32, (n - lo, 1), 0) + lo
            mult = jnp.where(sub > k, col * s, 0.0)
            m_ref[lo:, :] = m - mult * rk
            m_ref[pl.ds(k, 1), :] = rk
            return carry

        return step

    for g in range(n // GROUP):
        lax.fori_loop(g * GROUP, (g + 1) * GROUP, make_step(g * GROUP), 0)
    o_ref[...] = m_ref[:, n:]


def base_inv(a):
    n = a.shape[0]
    return pl.pallas_call(
        _base_kernel,
        out_shape=jax.ShapeDtypeStruct((n, n), jnp.float32),
        scratch_shapes=[pltpu.VMEM((n, 2 * n), jnp.float32)],
    )(a)


def chol_inv(a):
    n = a.shape[0]
    if n <= BASE:
        return base_inv(a)
    h = n // 2
    i11 = chol_inv(a[:h, :h])
    l21 = mmt(a[h:, :h], i11)
    i22 = chol_inv(a[h:, h:] - mmt(l21, l21))
    i21 = -mm(i22, mm(l21, i11))
    z = jnp.zeros((h, n - h), jnp.float32)
    return jnp.block([[i11, z], [i21, i22]])


def all_sum(g):
    n_dev = lax.axis_size("dev")
    n_grp = lax.axis_size("grp")
    rows, cols = g.shape
    part = lax.all_to_all(g.reshape(n_grp, rows // n_grp, cols), "grp", 0, 0, tiled=False).sum(0)
    piece = rows // (n_dev * n_grp)
    part = lax.all_to_all(part.reshape(n_dev, piece, cols), "dev", 0, 0, tiled=False).sum(0)
    part = jnp.broadcast_to(part[None], (n_dev,) + part.shape)
    part = lax.all_to_all(part, "dev", 0, 0, tiled=False).reshape(n_dev * piece, cols)
    return lax.all_gather(part, "grp", axis=0, tiled=True)


def shards(rows, lengths, sketch_block, sketch_sign):
    capacity = rows.shape[0]
    features = rows.shape[1]
    row_count = lengths.reshape(())
    slot_index = lax.iota(jnp.int32, capacity)
    is_live = slot_index < row_count
    row_sign = jnp.where(is_live, 2 * sketch_sign - 1, 0).astype(jnp.bfloat16)
    picker = (lax.iota(jnp.int32, SK_DEV)[:, None] == sketch_block[None, :]).astype(
        jnp.bfloat16
    ) * row_sign[None, :]
    sketched = jnp.dot(picker, rows, preferred_element_type=jnp.float32).astype(jnp.bfloat16)
    h = features // 2
    gram_left = all_sum(lax.dot_general(
        sketched, sketched[:, :h], (((0,), (0,)), ((), ())), preferred_element_type=jnp.float32
    ))
    gram_corner = all_sum(add_gram(sketched[:, h:]))
    ridge_value = float(lax.axis_size("grp") * lax.axis_size("dev") * MEAN)
    ridge = ridge_value * jnp.eye(h, dtype=jnp.float32)
    i11 = chol_inv(gram_left[:h] + ridge)
    l21 = mmt(gram_left[h:], i11)
    i22 = chol_inv(gram_corner + ridge - mmt(l21, l21))
    i21 = -mm(i22, mm(l21, i11))
    inverse = jnp.block([[i11, jnp.zeros((h, h), jnp.float32)], [i21, i22]])
    weight = inverse.T.astype(jnp.bfloat16)
    factor = ridge_value / features
    projected = jnp.dot(rows, weight, preferred_element_type=jnp.float32)
    return jnp.where(is_live, factor * jnp.sum(projected * projected, axis=1), 0.0)


def solution(mesh):
    in_specs = (P(("grp", "dev"), None), P("grp", "dev"), P(("grp", "dev")), P(("grp", "dev")))
    out_specs = P(("grp", "dev"))
    return jax.shard_map(shards, mesh=mesh, in_specs=in_specs, out_specs=out_specs, check_vma=False)
```

```python
import jax
import jax.numpy as jnp
from jax import lax
from jax.experimental import pallas as pl
from jax.experimental.pallas import tpu as pltpu
from jax.sharding import PartitionSpec as P

MEAN = 1024
SK_DEV = 512
BASE = 128
GROUP = 8
HI = lax.Precision.HIGHEST


def add_gram(row_piece):
    return lax.dot_general(
        row_piece, row_piece, (((0,), (0,)), ((), ())), preferred_element_type=jnp.float32
    )


def mm(a, b):
    return jnp.dot(a, b, precision=HI)


def mmt(a, b):
    return lax.dot_general(a, b, (((1,), (1,)), ((), ())), precision=HI)


def _base_kernel(a_ref, o_ref, m_ref):
    n = a_ref.shape[0]
    m_ref[:, :n] = a_ref[...]
    r = lax.broadcasted_iota(jnp.int32, (n, n), 0)
    c = lax.broadcasted_iota(jnp.int32, (n, n), 1)
    m_ref[:, n:] = jnp.where(r == c, 1.0, 0.0).astype(jnp.float32)

    def make_step(lo):
        def step(k, carry):
            row = m_ref[pl.ds(k, 1), :]
            lane = lax.broadcasted_iota(jnp.int32, (1, 2 * n), 1)
            piv = jnp.sum(jnp.where(lane == k, row, 0.0), axis=1, keepdims=True)
            s = lax.rsqrt(piv)
            rk = row * s
            m = m_ref[lo:, :]
            left_lane = lax.broadcasted_iota(jnp.int32, (n - lo, n), 1)
            col = jnp.sum(jnp.where(left_lane == k, m[:, :n], 0.0), axis=1, keepdims=True)
            sub = lax.broadcasted_iota(jnp.int32, (n - lo, 1), 0) + lo
            mult = jnp.where(sub > k, col * s, 0.0)
            m_ref[lo:, :] = m - mult * rk
            m_ref[pl.ds(k, 1), :] = rk
            return carry

        return step

    for g in range(n // GROUP):
        lax.fori_loop(g * GROUP, (g + 1) * GROUP, make_step(g * GROUP), 0)
    o_ref[...] = m_ref[:, n:]


def base_inv(a):
    n = a.shape[0]
    return pl.pallas_call(
        _base_kernel,
        out_shape=jax.ShapeDtypeStruct((n, n), jnp.float32),
        scratch_shapes=[pltpu.VMEM((n, 2 * n), jnp.float32)],
    )(a)


def chol_inv(a):
    n = a.shape[0]
    if n <= BASE:
        return base_inv(a)
    h = n // 2
    i11 = chol_inv(a[:h, :h])
    l21 = mmt(a[h:, :h], i11)
    i22 = chol_inv(a[h:, h:] - mmt(l21, l21))
    i21 = -mm(i22, mm(l21, i11))
    z = jnp.zeros((h, n - h), jnp.float32)
    return jnp.block([[i11, z], [i21, i22]])


def all_sum(left, corner):
    n_dev = lax.axis_size("dev")
    n_grp = lax.axis_size("grp")
    shapes = [x.shape for x in (left, corner)]
    chunks = [x.shape[0] // n_grp for x in (left, corner)]
    pieces = [c // n_dev for c in chunks]
    both = jnp.concatenate(
        [x.reshape(n_grp, c, x.shape[1]) for x, c in zip((left, corner), chunks)], axis=1
    )
    both = lax.all_to_all(both, "grp", 0, 0, tiled=False).sum(0)
    both = jnp.concatenate(
        [both[:chunks[0]].reshape(n_dev, pieces[0], -1), both[chunks[0]:].reshape(n_dev, pieces[1], -1)],
        axis=1,
    )
    both = lax.all_to_all(both, "dev", 0, 0, tiled=False).sum(0)
    both = jnp.broadcast_to(both[None], (n_dev,) + both.shape)
    both = lax.all_to_all(both, "dev", 0, 0, tiled=False)
    outs = []
    for part, piece, shape in ((both[:, :pieces[0]], pieces[0], shapes[0]), (both[:, pieces[0]:], pieces[1], shapes[1])):
        part = part.reshape(n_dev * piece, shape[1])
        outs.append(lax.all_gather(part, "grp", axis=0, tiled=True))
    return outs


def shards(rows, lengths, sketch_block, sketch_sign):
    capacity = rows.shape[0]
    features = rows.shape[1]
    row_count = lengths.reshape(())
    slot_index = lax.iota(jnp.int32, capacity)
    is_live = slot_index < row_count
    row_sign = jnp.where(is_live, 2 * sketch_sign - 1, 0).astype(jnp.bfloat16)
    picker = (lax.iota(jnp.int32, SK_DEV)[:, None] == sketch_block[None, :]).astype(
        jnp.bfloat16
    ) * row_sign[None, :]
    sketched = jnp.dot(picker, rows, preferred_element_type=jnp.float32).astype(jnp.bfloat16)
    h = features // 2
    gram_left, gram_corner = all_sum(
        lax.dot_general(
            sketched, sketched[:, :h], (((0,), (0,)), ((), ())), preferred_element_type=jnp.float32
        ),
        add_gram(sketched[:, h:]),
    )
    ridge_value = float(lax.axis_size("grp") * lax.axis_size("dev") * MEAN)
    ridge = ridge_value * jnp.eye(h, dtype=jnp.float32)
    i11 = chol_inv(gram_left[:h] + ridge)
    l21 = mmt(gram_left[h:], i11)
    i22 = chol_inv(gram_corner + ridge - mmt(l21, l21))
    i21 = -mm(i22, mm(l21, i11))
    inverse = jnp.block([[i11, jnp.zeros((h, h), jnp.float32)], [i21, i22]])
    weight = inverse.T.astype(jnp.bfloat16)
    factor = ridge_value / features
    projected = jnp.dot(rows, weight, preferred_element_type=jnp.float32)
    return jnp.where(is_live, factor * jnp.sum(projected * projected, axis=1), 0.0)


def solution(mesh):
    in_specs = (P(("grp", "dev"), None), P("grp", "dev"), P(("grp", "dev")), P(("grp", "dev")))
    out_specs = P(("grp", "dev"))
    return jax.shard_map(shards, mesh=mesh, in_specs=in_specs, out_specs=out_specs, check_vma=False)
```

```python
import jax
import jax.numpy as jnp
from jax import lax
from jax.experimental import pallas as pl
from jax.experimental.pallas import tpu as pltpu
from jax.sharding import PartitionSpec as P

MEAN = 1024
SK_DEV = 512
BASE = 128
GROUP = 8
HI = lax.Precision.HIGHEST


def add_gram(row_piece):
    return lax.dot_general(
        row_piece, row_piece, (((0,), (0,)), ((), ())), preferred_element_type=jnp.float32
    )


def mm(a, b):
    return jnp.dot(a, b, precision=HI)


def mmt(a, b):
    return lax.dot_general(a, b, (((1,), (1,)), ((), ())), precision=HI)


def _base_kernel(a_ref, o_ref, m_ref):
    n = a_ref.shape[0]
    m_ref[:, :n] = a_ref[...]
    r = lax.broadcasted_iota(jnp.int32, (n, n), 0)
    c = lax.broadcasted_iota(jnp.int32, (n, n), 1)
    m_ref[:, n:] = jnp.where(r == c, 1.0, 0.0).astype(jnp.float32)

    def make_step(lo):
        def step(k, carry):
            row = m_ref[pl.ds(k, 1), :]
            lane = lax.broadcasted_iota(jnp.int32, (1, 2 * n), 1)
            piv = jnp.sum(jnp.where(lane == k, row, 0.0), axis=1, keepdims=True)
            s = lax.rsqrt(piv)
            rk = row * s
            m = m_ref[lo:, :]
            left_lane = lax.broadcasted_iota(jnp.int32, (n - lo, n), 1)
            col = jnp.sum(jnp.where(left_lane == k, m[:, :n], 0.0), axis=1, keepdims=True)
            sub = lax.broadcasted_iota(jnp.int32, (n - lo, 1), 0) + lo
            mult = jnp.where(sub > k, col * s, 0.0)
            m_ref[lo:, :] = m - mult * rk
            m_ref[pl.ds(k, 1), :] = rk
            return carry

        return step

    for g in range(n // GROUP):
        lax.fori_loop(g * GROUP, (g + 1) * GROUP, make_step(g * GROUP), 0)
    o_ref[...] = m_ref[:, n:]


def base_inv(a):
    n = a.shape[0]
    return pl.pallas_call(
        _base_kernel,
        out_shape=jax.ShapeDtypeStruct((n, n), jnp.float32),
        scratch_shapes=[pltpu.VMEM((n, 2 * n), jnp.float32)],
    )(a)


def chol_inv(a):
    n = a.shape[0]
    if n <= BASE:
        return base_inv(a)
    h = n // 2
    i11 = chol_inv(a[:h, :h])
    l21 = mmt(a[h:, :h], i11)
    i22 = chol_inv(a[h:, h:] - mmt(l21, l21))
    i21 = -mm(i22, mm(l21, i11))
    z = jnp.zeros((h, n - h), jnp.float32)
    return jnp.block([[i11, z], [i21, i22]])


def all_sum(g):
    n_dev = lax.axis_size("dev")
    n_grp = lax.axis_size("grp")
    rows, cols = g.shape
    part = lax.all_to_all(g.reshape(n_grp, rows // n_grp, cols), "grp", 0, 0, tiled=False).sum(0)
    piece = rows // (n_dev * n_grp)
    part = lax.all_to_all(part.reshape(n_dev, piece, cols), "dev", 0, 0, tiled=False).sum(0)
    part = jnp.broadcast_to(part[None], (n_dev,) + part.shape)
    part = lax.all_to_all(part, "dev", 0, 0, tiled=False).reshape(n_dev * piece, cols)
    return lax.all_gather(part, "grp", axis=0, tiled=True)


def shards(rows, lengths, sketch_block, sketch_sign):
    capacity = rows.shape[0]
    features = rows.shape[1]
    row_count = lengths.reshape(())
    slot_index = lax.iota(jnp.int32, capacity)
    is_live = slot_index < row_count
    row_sign = jnp.where(is_live, 2 * sketch_sign - 1, 0).astype(jnp.bfloat16)
    picker = (lax.iota(jnp.int32, SK_DEV)[:, None] == sketch_block[None, :]).astype(
        jnp.bfloat16
    ) * row_sign[None, :]
    sketched = jnp.dot(picker, rows, preferred_element_type=jnp.float32).astype(jnp.bfloat16)
    h = features // 2
    gram_left = all_sum(lax.dot_general(
        sketched, sketched[:, :h], (((0,), (0,)), ((), ())), preferred_element_type=jnp.float32
    ))
    gram_corner = all_sum(add_gram(sketched[:, h:]))
    ridge_value = float(lax.axis_size("grp") * lax.axis_size("dev") * MEAN)
    ridge = ridge_value * jnp.eye(h, dtype=jnp.float32)
    i11 = chol_inv(gram_left[:h] + ridge)
    l21 = mmt(gram_left[h:], i11)
    i22 = chol_inv(gram_corner + ridge - mmt(l21, l21))
    i21 = -mm(i22, mm(l21, i11))
    w11, w12, w22 = (x.T.astype(jnp.bfloat16) for x in (i11, i21, i22))
    factor = ridge_value / features
    left = jnp.dot(rows[:, :h], w11, preferred_element_type=jnp.float32)
    right = jnp.dot(rows[:, :h], w12, preferred_element_type=jnp.float32) + jnp.dot(
        rows[:, h:], w22, preferred_element_type=jnp.float32
    )
    total = jnp.sum(left * left, axis=1) + jnp.sum(right * right, axis=1)
    return jnp.where(is_live, factor * total, 0.0)


def solution(mesh):
    in_specs = (P(("grp", "dev"), None), P("grp", "dev"), P(("grp", "dev")), P(("grp", "dev")))
    out_specs = P(("grp", "dev"))
    return jax.shard_map(shards, mesh=mesh, in_specs=in_specs, out_specs=out_specs, check_vma=False)
```

```python
import jax
import jax.numpy as jnp
from jax import lax
from jax.experimental import pallas as pl
from jax.experimental.pallas import tpu as pltpu
from jax.sharding import PartitionSpec as P

MEAN = 1024
SK_DEV = 512
BASE = 128
GROUP = 8
HI = lax.Precision.HIGHEST


def add_gram(row_piece):
    return lax.dot_general(
        row_piece, row_piece, (((0,), (0,)), ((), ())), preferred_element_type=jnp.float32
    )


def mm(a, b):
    return jnp.dot(a, b, precision=HI)


def mmt(a, b):
    return lax.dot_general(a, b, (((1,), (1,)), ((), ())), precision=HI)


def _base_kernel(a_ref, o_ref, m_ref):
    n = a_ref.shape[0]
    m_ref[:, :n] = a_ref[...]
    r = lax.broadcasted_iota(jnp.int32, (n, n), 0)
    c = lax.broadcasted_iota(jnp.int32, (n, n), 1)
    m_ref[:, n:] = jnp.where(r == c, 1.0, 0.0).astype(jnp.float32)

    def make_step(lo):
        def step(k, carry):
            row = m_ref[pl.ds(k, 1), :]
            lane = lax.broadcasted_iota(jnp.int32, (1, 2 * n), 1)
            piv = jnp.sum(jnp.where(lane == k, row, 0.0), axis=1, keepdims=True)
            s = lax.rsqrt(piv)
            rk = row * s
            m = m_ref[lo:, :]
            left_lane = lax.broadcasted_iota(jnp.int32, (n - lo, n), 1)
            col = jnp.sum(jnp.where(left_lane == k, m[:, :n], 0.0), axis=1, keepdims=True)
            sub = lax.broadcasted_iota(jnp.int32, (n - lo, 1), 0) + lo
            mult = jnp.where(sub > k, col * s, 0.0)
            m_ref[lo:, :] = m - mult * rk
            m_ref[pl.ds(k, 1), :] = rk
            return carry

        return step

    for g in range(n // GROUP):
        lax.fori_loop(g * GROUP, (g + 1) * GROUP, make_step(g * GROUP), 0)
    o_ref[...] = m_ref[:, n:]


def base_inv(a):
    n = BASE
    return pl.pallas_call(
        _base_kernel,
        out_shape=jax.ShapeDtypeStruct((n, n), jnp.float32),
        grid=(1,),
        in_specs=[pl.BlockSpec((n, n), lambda i: (0, 0))],
        out_specs=pl.BlockSpec((n, n), lambda i: (0, 0)),
        scratch_shapes=[pltpu.VMEM((n, 2 * n), jnp.float32)],
    )(a)


def chol_inv(a):
    n = a.shape[0]
    if n <= BASE:
        return base_inv(a)
    h = n // 2
    i11 = base_inv(a) if h <= BASE else chol_inv(a[:h, :h])
    l21 = mmt(a[h:, :h], i11)
    i22 = chol_inv(a[h:, h:] - mmt(l21, l21))
    i21 = -mm(i22, mm(l21, i11))
    z = jnp.zeros((h, n - h), jnp.float32)
    return jnp.block([[i11, z], [i21, i22]])


def all_sum(g):
    n_dev = lax.axis_size("dev")
    n_grp = lax.axis_size("grp")
    rows, cols = g.shape
    part = lax.all_to_all(g.reshape(n_grp, rows // n_grp, cols), "grp", 0, 0, tiled=False).sum(0)
    piece = rows // (n_dev * n_grp)
    part = lax.all_to_all(part.reshape(n_dev, piece, cols), "dev", 0, 0, tiled=False).sum(0)
    part = jnp.broadcast_to(part[None], (n_dev,) + part.shape)
    part = lax.all_to_all(part, "dev", 0, 0, tiled=False).reshape(n_dev * piece, cols)
    return lax.all_gather(part, "grp", axis=0, tiled=True)


def shards(rows, lengths, sketch_block, sketch_sign):
    capacity = rows.shape[0]
    features = rows.shape[1]
    row_count = lengths.reshape(())
    slot_index = lax.iota(jnp.int32, capacity)
    is_live = slot_index < row_count
    row_sign = jnp.where(is_live, 2 * sketch_sign - 1, 0).astype(jnp.bfloat16)
    picker = (lax.iota(jnp.int32, SK_DEV)[:, None] == sketch_block[None, :]).astype(
        jnp.bfloat16
    ) * row_sign[None, :]
    sketched = jnp.dot(picker, rows, preferred_element_type=jnp.float32).astype(jnp.bfloat16)
    h = features // 2
    gram_left = all_sum(lax.dot_general(
        sketched, sketched[:, :h], (((0,), (0,)), ((), ())), preferred_element_type=jnp.float32
    ))
    gram_corner = all_sum(add_gram(sketched[:, h:]))
    ridge_value = float(lax.axis_size("grp") * lax.axis_size("dev") * MEAN)
    ridge = ridge_value * jnp.eye(h, dtype=jnp.float32)
    i11 = chol_inv(gram_left[:h] + ridge)
    l21 = mmt(gram_left[h:], i11)
    i22 = chol_inv(gram_corner + ridge - mmt(l21, l21))
    i21 = -mm(i22, mm(l21, i11))
    inverse = jnp.block([[i11, jnp.zeros((h, h), jnp.float32)], [i21, i22]])
    weight = inverse.T.astype(jnp.bfloat16)
    factor = ridge_value / features
    projected = jnp.dot(rows, weight, preferred_element_type=jnp.float32)
    return jnp.where(is_live, factor * jnp.sum(projected * projected, axis=1), 0.0)


def solution(mesh):
    in_specs = (P(("grp", "dev"), None), P("grp", "dev"), P(("grp", "dev")), P(("grp", "dev")))
    out_specs = P(("grp", "dev"))
    return jax.shard_map(shards, mesh=mesh, in_specs=in_specs, out_specs=out_specs, check_vma=False)
```
